1024 devices in a mesh: dp: 32 (over z_hi, y), mp: 16 (over x, core), seq: 2 (over z_lo).
Axes of the slice: x: 8, y: 8, z: 8 (z_hi: 4, z_lo: 2; z = z_hi * 2 + z_lo), core: 2. Of those that a mesh axis runs over, the one named last changes fastest.
Arguments:
- queries: bfloat16 [64, 256, 6144], P(('dp', 'seq'), None, 'mp'), may hold values from -20 to 20
- key_rows: bfloat16 [64, 256, 6144], P(('dp', 'seq'), None, 'mp'), may hold values from -12 to 12
- value_rows: bfloat16 [64, 256, 6144], P(('dp', 'seq'), None, 'mp'), may hold values from -6 to 6
- projection: bfloat16 [6144, 4096], P('mp', ('dp', 'seq')), may hold values from -0.21875 to 0.21875
- upstream: bfloat16 [256, 64, 4096], P('mp', ('dp', 'seq')), may hold values from -6 to 6
Outputs:
- projected: bfloat16 [256, 64, 4096], P('mp', ('dp', 'seq'))
- grad_queries: float32 [64, 256, 6144], P(('dp', 'seq'), None, 'mp')
- grad_keys: float32 [64, 256, 6144], P(('dp', 'seq'), None, 'mp')
- grad_values: float32 [64, 256, 6144], P(('dp', 'seq'), None, 'mp')
The draws below stay inside these ranges and needn't reach their ends.
All inputs are finite; a program needn't handle non-finite values.
Results may differ from the reference program's by a relative error of at most 0.023.
Values may be sent and summed in bfloat16 or wider, within the bound.
No kernel may reach another device: no remote copies, remote signals or barrier semaphores. Data moves between devices by JAX's collectives and lax.ppermute only.
A program may use at most 32 MiB of HBM per device.

```python
import math
import jax
import jax.numpy as jnp
from jax import lax

D_VIT = 6144
HEADS = 48
HEAD_DIM = 128
D_LM = 4096
PATCHES = 256
FRAMES = 64
N_MP = 16


def draw_pair(key):
    query_key, other_key = jax.random.split(jax.random.fold_in(key, 11))
    shape = (FRAMES, PATCHES, D_VIT)
    query_draw = jnp.clip(jax.random.normal(query_key, shape, jnp.float32), -6.0, 6.0)
    key_draw = jnp.clip(2.0 * jax.random.normal(other_key, shape, jnp.float32), -12.0, 12.0)
    return (query_draw, key_draw)


def draw_queries(key, part):
    return draw_pair(key)[0].astype(jnp.bfloat16)


def draw_key_rows(key, part):
    return draw_pair(key)[1].astype(jnp.bfloat16)


def level_of(own_key, extent, cuts, smallest, largest):
    def one(axis_at, shards_of):
        steps = jax.random.uniform(jax.random.fold_in(jax.random.fold_in(own_key, 6), axis_at), (shards_of,), jnp.float32, smallest / len(cuts), largest / len(cuts))
        return jnp.repeat(jnp.exp(steps), extent[axis_at] // shards_of).reshape((-1,) + (1,) * (len(extent) - axis_at - 1))

    level = one(*cuts[0])
    for cut in cuts[1:]:
        level = level * one(*cut)
    return level


def scatter_about(key, shape, spread, limit, cuts=(), kind=jnp.bfloat16):
    values = spread * jax.random.normal(key, shape, jnp.float32)
    if cuts:
        values = values * level_of(key, shape, cuts, -0.22, 0.18)
    return jnp.clip(values, -limit, limit).astype(kind)


def setup_inputs(seed: int = 0) -> dict:
    streams_of = jax.random.split(jax.random.key(seed), 6)
    return {
        "queries": draw_queries(jax.random.fold_in(streams_of[5], 71), 0),
        "key_rows": draw_key_rows(jax.random.fold_in(streams_of[5], 71), 0),
        "value_rows": scatter_about(streams_of[2], (FRAMES, PATCHES, D_VIT), 1.0, 6.0, ((0, 64), (2, 16))),
        "projection": scatter_about(streams_of[3], (D_VIT, D_LM), (D_VIT // 8) ** -0.5, 0.21875, ((0, 16), (1, 64))),
        "upstream": scatter_about(streams_of[4], (PATCHES, FRAMES, D_LM), 1.0, 6.0, ((0, 16), (1, 64))),
    }


def split_heads(block):
    return block.astype(jnp.float32).reshape(PATCHES, HEADS, HEAD_DIM)

def frame_soft(query_block, key_block):
    factor = 1.0 / math.sqrt(HEAD_DIM)
    scores = jnp.einsum('qhd,khd->hqk', split_heads(query_block), split_heads(key_block)) * factor
    return jax.nn.softmax(scores, axis=-1)

def frame_forward(blocks):
    query_block, key_block, value_block = blocks
    soft = frame_soft(query_block, key_block)
    soft_b = lax.optimization_barrier(soft.astype(jnp.bfloat16)).astype(jnp.float32)
    attended = jnp.einsum('hqk,khd->qhd', soft_b, split_heads(value_block)).astype(jnp.bfloat16)
    return attended.reshape(PATCHES, D_VIT)

def frame_backward(blocks):
    query_block, key_block, value_block, grad_block = blocks
    factor = 1.0 / math.sqrt(HEAD_DIM)
    soft = frame_soft(query_block, key_block)
    soft_b = lax.optimization_barrier(soft.astype(jnp.bfloat16)).astype(jnp.float32)
    grad_heads = split_heads(grad_block)
    grad_soft = jnp.einsum('qhd,khd->hqk', grad_heads, split_heads(value_block))
    inner_sum = lax.optimization_barrier(jnp.sum(grad_soft * soft, axis=-1, keepdims=True))
    grad_scores = soft * (grad_soft - inner_sum)
    grad_scores = lax.optimization_barrier(grad_scores.astype(jnp.bfloat16)).astype(jnp.float32)
    grad_q = jnp.einsum('hqk,khd->qhd', grad_scores, split_heads(key_block)) * factor
    grad_k = jnp.einsum('hqk,qhd->khd', grad_scores, split_heads(query_block)) * factor
    grad_v = jnp.einsum('hqk,qhd->khd', soft_b, grad_heads)
    return (grad_q.reshape(PATCHES, D_VIT), grad_k.reshape(PATCHES, D_VIT), grad_v.reshape(PATCHES, D_VIT))

def reference(queries, key_rows, value_rows, projection, upstream):
    attended = lax.map(frame_forward, (queries, key_rows, value_rows))
    tokens = attended.reshape(FRAMES * PATCHES, D_VIT)
    block_width = D_VIT // N_MP

    def add_block(running, group):
        row_block = lax.dynamic_slice_in_dim(tokens, group * block_width, block_width, 1)
        weight_block = lax.dynamic_slice_in_dim(projection, group * block_width, block_width, 0)
        partial_value = jnp.dot(row_block, weight_block, preferred_element_type=jnp.float32)
        partial_value = lax.optimization_barrier(partial_value.astype(jnp.bfloat16)).astype(jnp.float32)
        return (running + partial_value, None)
    zeros = jnp.zeros((FRAMES * PATCHES, D_LM), jnp.float32)
    total, _ = lax.scan(add_block, zeros, jnp.arange(N_MP, dtype=jnp.int32))
    projected = total.astype(jnp.bfloat16).reshape(FRAMES, PATCHES, D_LM).transpose(1, 0, 2)
    grad_tokens = upstream.transpose(1, 0, 2).reshape(FRAMES * PATCHES, D_LM)
    grad_attended = jnp.dot(grad_tokens, projection.T, preferred_element_type=jnp.float32)
    grad_attended = grad_attended.astype(jnp.bfloat16).reshape(FRAMES, PATCHES, D_VIT)
    grad_queries, grad_keys, grad_values = lax.map(frame_backward, (queries, key_rows, value_rows, grad_attended))
    return (projected, grad_queries, grad_keys, grad_values)
```

```python
import math

import jax
import jax.numpy as jnp
from jax import lax
from jax.sharding import Mesh, PartitionSpec as P

HEADS = 48


def split_heads(block, head_count):
    frame_count, row_count, feature_count = block.shape
    return block.reshape(frame_count, row_count, head_count, feature_count // head_count)


def soft_weights(queries, key_rows, head_count):
    split_q = split_heads(queries, head_count)
    factor = 1.0 / math.sqrt(split_q.shape[3])
    scores = (
        jnp.einsum(
            "fqhd,fkhd->fhqk",
            split_q,
            split_heads(key_rows, head_count),
            preferred_element_type=jnp.float32,
        )
        * factor
    )
    return jax.nn.softmax(scores, axis=-1)


def attend_values(soft, value_rows, head_count):
    mixed = jnp.einsum(
        "fhqk,fkhd->fqhd",
        soft.astype(jnp.bfloat16),
        split_heads(value_rows, head_count),
        preferred_element_type=jnp.float32,
    )
    frame_count, row_count = (mixed.shape[0], mixed.shape[1])
    return mixed.astype(jnp.bfloat16).reshape(frame_count, row_count, -1)


def backward_heads(soft, queries, key_rows, value_rows, grad_attended, head_count):
    split_q = split_heads(queries, head_count)
    split_k = split_heads(key_rows, head_count)
    split_v = split_heads(value_rows, head_count)
    split_g = split_heads(grad_attended, head_count)
    factor = 1.0 / math.sqrt(split_q.shape[3])
    grad_soft = jnp.einsum("fqhd,fkhd->fhqk", split_g, split_v, preferred_element_type=jnp.float32)
    inner_sum = jnp.sum(grad_soft * soft, axis=-1, keepdims=True)
    grad_scores = (soft * (grad_soft - inner_sum)).astype(jnp.bfloat16)
    grad_q = (
        jnp.einsum("fhqk,fkhd->fqhd", grad_scores, split_k, preferred_element_type=jnp.float32)
        * factor
    )
    grad_k = (
        jnp.einsum("fhqk,fqhd->fkhd", grad_scores, split_q, preferred_element_type=jnp.float32)
        * factor
    )
    grad_v = jnp.einsum(
        "fhqk,fqhd->fkhd", soft.astype(jnp.bfloat16), split_g, preferred_element_type=jnp.float32
    )
    return (
        grad_q.reshape(queries.shape),
        grad_k.reshape(key_rows.shape),
        grad_v.reshape(value_rows.shape),
    )


def gather_columns(projection):
    along_z = lax.all_gather(projection, ("zh", "zl"), axis=1, tiled=True)
    along_yz = lax.all_gather(along_z, "y", axis=1, tiled=True)
    rows, width = projection.shape
    ys, zhs, zls = (lax.axis_size(a) for a in ("y", "zh", "zl"))
    blocks = along_yz.reshape(rows, ys, zhs, zls, width)
    return blocks.transpose(0, 2, 1, 3, 4).reshape(rows, -1)


def on_device(queries, key_rows, value_rows, projection, upstream):
    head_count = HEADS // (lax.axis_size("x") * lax.axis_size("c"))
    soft = soft_weights(queries, key_rows, head_count)
    attended = attend_values(soft, value_rows, head_count)
    ordered = attended.transpose(1, 0, 2)
    grad_full = lax.all_gather(upstream, ("x", "c"), axis=0, tiled=True)
    columns = gather_columns(projection)
    grad_attended = jnp.einsum(
        "qfd,cd->fqc", grad_full, columns, preferred_element_type=jnp.float32
    )
    partial = jnp.einsum(
        "qfc,cd->qfd", ordered, columns, preferred_element_type=jnp.float32
    ).astype(jnp.bfloat16)
    projected = lax.psum_scatter(partial, "x", scatter_dimension=0, tiled=True)
    projected = lax.psum_scatter(projected, "c", scatter_dimension=0, tiled=True)
    grad_rounded = grad_attended.astype(jnp.bfloat16)
    grad_q, grad_k, grad_v = backward_heads(
        soft, queries, key_rows, value_rows, grad_rounded, head_count
    )
    return (projected, grad_q, grad_k, grad_v)


def fine_mesh(mesh):
    devices = mesh.devices
    dp, mp, seq = devices.shape
    ys = len({d.coords[1] for d in devices[:, 0, 0]}) if hasattr(devices[0, 0, 0], "coords") else dp
    shape = (dp // ys, ys, mp // 2, 2, seq)
    return Mesh(devices.reshape(shape), ("zh", "y", "x", "c", "zl"))


def solution(mesh):
    fine = fine_mesh(mesh)
    frames = ("zh", "y", "zl")
    heads = ("x", "c")
    return jax.shard_map(
        on_device,
        mesh=fine,
        in_specs=(
            P(frames, None, heads),
            P(frames, None, heads),
            P(frames, None, heads),
            P(heads, frames),
            P(heads, frames, None),
        ),
        out_specs=(
            P(heads, frames, None),
            P(frames, None, heads),
            P(frames, None, heads),
            P(frames, None, heads),
        ),
        check_vma=False,
    )
```

```python
import math

import jax
import jax.numpy as jnp
from jax import lax
from jax.sharding import Mesh, PartitionSpec as P

HEADS = 48


def split_heads(block, head_count):
    frame_count, row_count, feature_count = block.shape
    return block.reshape(frame_count, row_count, head_count, feature_count // head_count)


def soft_weights(queries, key_rows, head_count):
    split_q = split_heads(queries, head_count)
    factor = 1.0 / math.sqrt(split_q.shape[3])
    scores = (
        jnp.einsum(
            "fqhd,fkhd->fhqk",
            split_q,
            split_heads(key_rows, head_count),
            preferred_element_type=jnp.float32,
        )
        * factor
    )
    return jax.nn.softmax(scores, axis=-1)


def attend_values(soft, value_rows, head_count):
    mixed = jnp.einsum(
        "fhqk,fkhd->fqhd",
        soft.astype(jnp.bfloat16),
        split_heads(value_rows, head_count),
        preferred_element_type=jnp.float32,
    )
    frame_count, row_count = (mixed.shape[0], mixed.shape[1])
    return mixed.astype(jnp.bfloat16).reshape(frame_count, row_count, -1)


def backward_heads(soft, queries, key_rows, value_rows, grad_attended, head_count):
    split_q = split_heads(queries, head_count)
    split_k = split_heads(key_rows, head_count)
    split_v = split_heads(value_rows, head_count)
    split_g = split_heads(grad_attended, head_count)
    factor = 1.0 / math.sqrt(split_q.shape[3])
    grad_soft = jnp.einsum("fqhd,fkhd->fhqk", split_g, split_v, preferred_element_type=jnp.float32)
    inner_sum = jnp.sum(grad_soft * soft, axis=-1, keepdims=True)
    grad_scores = (soft * (grad_soft - inner_sum)).astype(jnp.bfloat16)
    grad_q = (
        jnp.einsum("fhqk,fkhd->fqhd", grad_scores, split_k, preferred_element_type=jnp.float32)
        * factor
    )
    grad_k = (
        jnp.einsum("fhqk,fqhd->fkhd", grad_scores, split_q, preferred_element_type=jnp.float32)
        * factor
    )
    grad_v = jnp.einsum(
        "fhqk,fqhd->fkhd", soft.astype(jnp.bfloat16), split_g, preferred_element_type=jnp.float32
    )
    return (
        grad_q.reshape(queries.shape),
        grad_k.reshape(key_rows.shape),
        grad_v.reshape(value_rows.shape),
    )


def gather_columns(projection):
    along_z = lax.all_gather(projection, ("zh", "zl"), axis=1, tiled=True)
    along_yz = lax.all_gather(along_z, "y", axis=1, tiled=True)
    rows, width = projection.shape
    ys, zhs, zls = (lax.axis_size(a) for a in ("y", "zh", "zl"))
    blocks = along_yz.reshape(rows, ys, zhs, zls, width)
    return blocks.transpose(0, 2, 1, 3, 4).reshape(rows, -1)


def sum_patch_blocks(partial):
    groups = lax.axis_size("x") * lax.axis_size("c")
    blocks = partial.reshape(groups, partial.shape[0] // groups, *partial.shape[1:])
    received = lax.all_to_all(blocks, ("x", "c"), 0, 0, tiled=False)
    return received.astype(jnp.float32).sum(axis=0).astype(jnp.bfloat16)


def on_device(queries, key_rows, value_rows, projection, upstream):
    head_count = HEADS // (lax.axis_size("x") * lax.axis_size("c"))
    soft = soft_weights(queries, key_rows, head_count)
    attended = attend_values(soft, value_rows, head_count)
    ordered = attended.transpose(1, 0, 2)
    grad_full = lax.all_gather(upstream, ("x", "c"), axis=0, tiled=True)
    columns = gather_columns(projection)
    grad_attended = jnp.einsum(
        "qfd,cd->fqc", grad_full, columns, preferred_element_type=jnp.float32
    )
    partial = jnp.einsum(
        "qfc,cd->qfd", ordered, columns, preferred_element_type=jnp.float32
    ).astype(jnp.bfloat16)
    projected = sum_patch_blocks(partial)
    grad_rounded = grad_attended.astype(jnp.bfloat16)
    grad_q, grad_k, grad_v = backward_heads(
        soft, queries, key_rows, value_rows, grad_rounded, head_count
    )
    return (projected, grad_q, grad_k, grad_v)


def fine_mesh(mesh):
    devices = mesh.devices
    dp, mp, seq = devices.shape
    ys = len({d.coords[1] for d in devices[:, 0, 0]}) if hasattr(devices[0, 0, 0], "coords") else dp
    shape = (dp // ys, ys, mp // 2, 2, seq)
    return Mesh(devices.reshape(shape), ("zh", "y", "x", "c", "zl"))


def solution(mesh):
    fine = fine_mesh(mesh)
    frames = ("zh", "y", "zl")
    heads = ("x", "c")
    return jax.shard_map(
        on_device,
        mesh=fine,
        in_specs=(
            P(frames, None, heads),
            P(frames, None, heads),
            P(frames, None, heads),
            P(heads, frames),
            P(heads, frames, None),
        ),
        out_specs=(
            P(heads, frames, None),
            P(frames, None, heads),
            P(frames, None, heads),
            P(frames, None, heads),
        ),
        check_vma=False,
    )
```

```python
import math

import jax
import jax.numpy as jnp
from jax import lax
from jax.sharding import Mesh, PartitionSpec as P

HEADS = 48


def split_heads(block, head_count):
    frame_count, row_count, feature_count = block.shape
    return block.reshape(frame_count, row_count, head_count, feature_count // head_count)


def soft_weights(queries, key_rows, head_count):
    split_q = split_heads(queries, head_count)
    factor = 1.0 / math.sqrt(split_q.shape[3])
    scores = (
        jnp.einsum(
            "fqhd,fkhd->fhqk",
            split_q,
            split_heads(key_rows, head_count),
            preferred_element_type=jnp.float32,
        )
        * factor
    )
    return jax.nn.softmax(scores, axis=-1)


def attend_values(soft, value_rows, head_count):
    mixed = jnp.einsum(
        "fhqk,fkhd->fqhd",
        soft.astype(jnp.bfloat16),
        split_heads(value_rows, head_count),
        preferred_element_type=jnp.float32,
    )
    frame_count, row_count = (mixed.shape[0], mixed.shape[1])
    return mixed.astype(jnp.bfloat16).reshape(frame_count, row_count, -1)


def backward_heads(soft, queries, key_rows, value_rows, grad_attended, head_count):
    split_q = split_heads(queries, head_count)
    split_k = split_heads(key_rows, head_count)
    split_v = split_heads(value_rows, head_count)
    split_g = split_heads(grad_attended, head_count)
    factor = 1.0 / math.sqrt(split_q.shape[3])
    grad_soft = jnp.einsum("fqhd,fkhd->fhqk", split_g, split_v, preferred_element_type=jnp.float32)
    inner_sum = jnp.sum(grad_soft * soft, axis=-1, keepdims=True)
    grad_scores = (soft * (grad_soft - inner_sum)).astype(jnp.bfloat16)
    grad_q = (
        jnp.einsum("fhqk,fkhd->fqhd", grad_scores, split_k, preferred_element_type=jnp.float32)
        * factor
    )
    grad_k = (
        jnp.einsum("fhqk,fqhd->fkhd", grad_scores, split_q, preferred_element_type=jnp.float32)
        * factor
    )
    grad_v = jnp.einsum(
        "fhqk,fqhd->fkhd", soft.astype(jnp.bfloat16), split_g, preferred_element_type=jnp.float32
    )
    return (
        grad_q.reshape(queries.shape),
        grad_k.reshape(key_rows.shape),
        grad_v.reshape(value_rows.shape),
    )


def gather_columns(projection):
    along_z = lax.all_gather(projection, ("zh", "zl"), axis=1, tiled=True)
    along_yz = lax.all_gather(along_z, "y", axis=1, tiled=True)
    rows, width = projection.shape
    ys, zhs, zls = (lax.axis_size(a) for a in ("y", "zh", "zl"))
    blocks = along_yz.reshape(rows, ys, zhs, zls, width)
    return blocks.transpose(0, 2, 1, 3, 4).reshape(rows, -1)


def gather_patch_blocks(upstream):
    groups = lax.axis_size("x") * lax.axis_size("c")
    copies = jnp.broadcast_to(upstream[None], (groups,) + upstream.shape)
    received = lax.all_to_all(copies, ("x", "c"), 0, 0, tiled=False)
    return received.reshape(groups * upstream.shape[0], *upstream.shape[1:])


def sum_patch_blocks(partial):
    groups = lax.axis_size("x") * lax.axis_size("c")
    blocks = partial.reshape(groups, partial.shape[0] // groups, *partial.shape[1:])
    received = lax.all_to_all(blocks, ("x", "c"), 0, 0, tiled=False)
    return received.astype(jnp.float32).sum(axis=0).astype(jnp.bfloat16)


def on_device(queries, key_rows, value_rows, projection, upstream):
    head_count = HEADS // (lax.axis_size("x") * lax.axis_size("c"))
    soft = soft_weights(queries, key_rows, head_count)
    attended = attend_values(soft, value_rows, head_count)
    ordered = attended.transpose(1, 0, 2)
    grad_full = gather_patch_blocks(upstream)
    columns = gather_columns(projection)
    grad_attended = jnp.einsum(
        "qfd,cd->fqc", grad_full, columns, preferred_element_type=jnp.float32
    )
    partial = jnp.einsum(
        "qfc,cd->qfd", ordered, columns, preferred_element_type=jnp.float32
    ).astype(jnp.bfloat16)
    projected = sum_patch_blocks(partial)
    grad_rounded = grad_attended.astype(jnp.bfloat16)
    grad_q, grad_k, grad_v = backward_heads(
        soft, queries, key_rows, value_rows, grad_rounded, head_count
    )
    return (projected, grad_q, grad_k, grad_v)


def fine_mesh(mesh):
    devices = mesh.devices
    dp, mp, seq = devices.shape
    ys = len({d.coords[1] for d in devices[:, 0, 0]}) if hasattr(devices[0, 0, 0], "coords") else dp
    shape = (dp // ys, ys, mp // 2, 2, seq)
    return Mesh(devices.reshape(shape), ("zh", "y", "x", "c", "zl"))


def solution(mesh):
    fine = fine_mesh(mesh)
    frames = ("zh", "y", "zl")
    heads = ("x", "c")
    return jax.shard_map(
        on_device,
        mesh=fine,
        in_specs=(
            P(frames, None, heads),
            P(frames, None, heads),
            P(frames, None, heads),
            P(heads, frames),
            P(heads, frames, None),
        ),
        out_specs=(
            P(heads, frames, None),
            P(frames, None, heads),
            P(frames, None, heads),
            P(frames, None, heads),
        ),
        check_vma=False,
    )
```

```python
import math

import jax
import jax.numpy as jnp
from jax import lax
from jax.sharding import Mesh, PartitionSpec as P

HEADS = 48


def split_heads(block, head_count):
    frame_count, row_count, feature_count = block.shape
    return block.reshape(frame_count, row_count, head_count, feature_count // head_count)


def soft_weights(queries, key_rows, head_count):
    split_q = split_heads(queries, head_count)
    factor = 1.0 / math.sqrt(split_q.shape[3])
    scores = (
        jnp.einsum(
            "fqhd,fkhd->fhqk",
            split_q,
            split_heads(key_rows, head_count),
            preferred_element_type=jnp.float32,
        )
        * factor
    )
    return jax.nn.softmax(scores, axis=-1)


def attend_values(soft, value_rows, head_count):
    mixed = jnp.einsum(
        "fhqk,fkhd->fqhd",
        soft.astype(jnp.bfloat16),
        split_heads(value_rows, head_count),
        preferred_element_type=jnp.float32,
    )
    frame_count, row_count = (mixed.shape[0], mixed.shape[1])
    return mixed.astype(jnp.bfloat16).reshape(frame_count, row_count, -1)


def backward_heads(soft, queries, key_rows, value_rows, grad_attended, head_count):
    split_q = split_heads(queries, head_count)
    split_k = split_heads(key_rows, head_count)
    split_v = split_heads(value_rows, head_count)
    split_g = split_heads(grad_attended, head_count)
    factor = 1.0 / math.sqrt(split_q.shape[3])
    grad_soft = jnp.einsum("fqhd,fkhd->fhqk", split_g, split_v, preferred_element_type=jnp.float32)
    inner_sum = jnp.sum(grad_soft * soft, axis=-1, keepdims=True)
    grad_scores = (soft * (grad_soft - inner_sum)).astype(jnp.bfloat16)
    grad_q = (
        jnp.einsum("fhqk,fkhd->fqhd", grad_scores, split_k, preferred_element_type=jnp.float32)
        * factor
    )
    grad_k = (
        jnp.einsum("fhqk,fqhd->fkhd", grad_scores, split_q, preferred_element_type=jnp.float32)
        * factor
    )
    grad_v = jnp.einsum(
        "fhqk,fqhd->fkhd", soft.astype(jnp.bfloat16), split_g, preferred_element_type=jnp.float32
    )
    return (
        grad_q.reshape(queries.shape),
        grad_k.reshape(key_rows.shape),
        grad_v.reshape(value_rows.shape),
    )


def gather_columns(projection):
    along_z = lax.all_gather(projection, ("zh", "zl"), axis=1, tiled=True)
    along_yz = lax.all_gather(along_z, "y", axis=1, tiled=True)
    rows, width = projection.shape
    ys, zhs, zls = (lax.axis_size(a) for a in ("y", "zh", "zl"))
    blocks = along_yz.reshape(rows, ys, zhs, zls, width)
    return blocks.transpose(0, 2, 1, 3, 4).reshape(rows, -1)


def swap_cores(block):
    return lax.ppermute(block, "c", [(0, 1), (1, 0)])


def gather_patch_blocks(upstream):
    chips = lax.axis_size("x")
    copies = jnp.broadcast_to(upstream[None], (chips,) + upstream.shape)
    mine = lax.all_to_all(copies, "x", 0, 0, tiled=False)
    other = swap_cores(mine)
    first = lax.axis_index("c") == 0
    both = jnp.stack([jnp.where(first, mine, other), jnp.where(first, other, mine)], axis=1)
    return both.reshape(chips * 2 * upstream.shape[0], *upstream.shape[1:])


def sum_patch_blocks(partial):
    chips = lax.axis_size("x")
    blocks = partial.reshape(chips, 2, partial.shape[0] // (2 * chips), *partial.shape[1:])
    core = lax.axis_index("c")
    keep = lax.dynamic_index_in_dim(blocks, core, axis=1, keepdims=False)
    send = lax.dynamic_index_in_dim(blocks, 1 - core, axis=1, keepdims=False)
    pair = (keep.astype(jnp.float32) + swap_cores(send).astype(jnp.float32)).astype(jnp.bfloat16)
    received = lax.all_to_all(pair, "x", 0, 0, tiled=False)
    return received.astype(jnp.float32).sum(axis=0).astype(jnp.bfloat16)


def on_device(queries, key_rows, value_rows, projection, upstream):
    head_count = HEADS // (lax.axis_size("x") * lax.axis_size("c"))
    soft = soft_weights(queries, key_rows, head_count)
    attended = attend_values(soft, value_rows, head_count)
    ordered = attended.transpose(1, 0, 2)
    grad_full = gather_patch_blocks(upstream)
    columns = gather_columns(projection)
    grad_attended = jnp.einsum(
        "qfd,cd->fqc", grad_full, columns, preferred_element_type=jnp.float32
    )
    partial = jnp.einsum(
        "qfc,cd->qfd", ordered, columns, preferred_element_type=jnp.float32
    ).astype(jnp.bfloat16)
    projected = sum_patch_blocks(partial)
    grad_rounded = grad_attended.astype(jnp.bfloat16)
    grad_q, grad_k, grad_v = backward_heads(
        soft, queries, key_rows, value_rows, grad_rounded, head_count
    )
    return (projected, grad_q, grad_k, grad_v)


def fine_mesh(mesh):
    devices = mesh.devices
    dp, mp, seq = devices.shape
    ys = len({d.coords[1] for d in devices[:, 0, 0]}) if hasattr(devices[0, 0, 0], "coords") else dp
    shape = (dp // ys, ys, mp // 2, 2, seq)
    return Mesh(devices.reshape(shape), ("zh", "y", "x", "c", "zl"))


def solution(mesh):
    fine = fine_mesh(mesh)
    frames = ("zh", "y", "zl")
    heads = ("x", "c")
    return jax.shard_map(
        on_device,
        mesh=fine,
        in_specs=(
            P(frames, None, heads),
            P(frames, None, heads),
            P(frames, None, heads),
            P(heads, frames),
            P(heads, frames, None),
        ),
        out_specs=(
            P(heads, frames, None),
            P(frames, None, heads),
            P(frames, None, heads),
            P(frames, None, heads),
        ),
        check_vma=False,
    )
```

```python
import math

import jax
import jax.numpy as jnp
from jax import lax
from jax.sharding import Mesh, PartitionSpec as P

HEADS = 48


def split_heads(block, head_count):
    frame_count, row_count, feature_count = block.shape
    return block.reshape(frame_count, row_count, head_count, feature_count // head_count)


def soft_weights(queries, key_rows, head_count):
    split_q = split_heads(queries, head_count)
    factor = 1.0 / math.sqrt(split_q.shape[3])
    scores = (
        jnp.einsum(
            "fqhd,fkhd->fhqk",
            split_q,
            split_heads(key_rows, head_count),
            preferred_element_type=jnp.float32,
        )
        * factor
    )
    return jax.nn.softmax(scores, axis=-1)


def attend_values(soft, value_rows, head_count):
    mixed = jnp.einsum(
        "fhqk,fkhd->fqhd",
        soft.astype(jnp.bfloat16),
        split_heads(value_rows, head_count),
        preferred_element_type=jnp.float32,
    )
    frame_count, row_count = (mixed.shape[0], mixed.shape[1])
    return mixed.astype(jnp.bfloat16).reshape(frame_count, row_count, -1)


def backward_heads(soft, queries, key_rows, value_rows, grad_attended, head_count):
    split_q = split_heads(queries, head_count)
    split_k = split_heads(key_rows, head_count)
    split_v = split_heads(value_rows, head_count)
    split_g = split_heads(grad_attended, head_count)
    factor = 1.0 / math.sqrt(split_q.shape[3])
    grad_soft = jnp.einsum("fqhd,fkhd->fhqk", split_g, split_v, preferred_element_type=jnp.float32)
    inner_sum = jnp.sum(grad_soft * soft, axis=-1, keepdims=True)
    grad_scores = (soft * (grad_soft - inner_sum)).astype(jnp.bfloat16)
    grad_q = (
        jnp.einsum("fhqk,fkhd->fqhd", grad_scores, split_k, preferred_element_type=jnp.float32)
        * factor
    )
    grad_k = (
        jnp.einsum("fhqk,fqhd->fkhd", grad_scores, split_q, preferred_element_type=jnp.float32)
        * factor
    )
    grad_v = jnp.einsum(
        "fhqk,fqhd->fkhd", soft.astype(jnp.bfloat16), split_g, preferred_element_type=jnp.float32
    )
    return (
        grad_q.reshape(queries.shape),
        grad_k.reshape(key_rows.shape),
        grad_v.reshape(value_rows.shape),
    )


def swap_cores(block):
    return lax.ppermute(block, "c", [(0, 1), (1, 0)])


def gather_by_all_to_all(block, axis):
    count = lax.axis_size(axis)
    copies = jnp.broadcast_to(block[None], (count,) + block.shape)
    return lax.all_to_all(copies, axis, 0, 0, tiled=False)


def gather_patch_blocks(pieces):
    chips = lax.axis_size("x")
    mine = gather_by_all_to_all(pieces, "x")
    other = swap_cores(mine)
    first = lax.axis_index("c") == 0
    both = jnp.stack([jnp.where(first, mine, other), jnp.where(first, other, mine)], axis=1)
    return both.reshape(chips * 2 * pieces.shape[0], *pieces.shape[1:])


def sum_patch_blocks(blocks):
    core = lax.axis_index("c")
    keep = lax.dynamic_index_in_dim(blocks, core, axis=1, keepdims=False)
    send = lax.dynamic_index_in_dim(blocks, 1 - core, axis=1, keepdims=False)
    pair = (keep.astype(jnp.float32) + swap_cores(send).astype(jnp.float32)).astype(jnp.bfloat16)
    received = lax.all_to_all(pair, "x", 0, 0, tiled=False)
    return received.astype(jnp.float32).sum(axis=0).astype(jnp.bfloat16)


def on_device(queries, key_rows, value_rows, projection, upstream):
    chips, ys = lax.axis_size("x"), lax.axis_size("y")
    zhs, zls = lax.axis_size("zh"), lax.axis_size("zl")
    head_count = HEADS // (chips * 2)
    soft = soft_weights(queries, key_rows, head_count)
    attended = attend_values(soft, value_rows, head_count)
    patches, width = attended.shape[1], attended.shape[2]
    block = patches // (chips * 2)
    columns = lax.all_gather(projection, ("zh", "zl"), axis=1, tiled=True)
    span = columns.shape[1]
    group = gather_by_all_to_all(attended[0], "y")
    tokens = group.reshape(ys, chips, 2, block, width)
    partial = jnp.einsum(
        "gxcpf,fd->xcgpd", tokens, columns, preferred_element_type=jnp.float32
    ).astype(jnp.bfloat16)
    summed = sum_patch_blocks(partial)
    own = lax.all_to_all(summed, "y", 0, 0, tiled=False)
    projected = (
        own.reshape(ys, block, zhs, zls, span // (zhs * zls))
        .transpose(1, 2, 0, 3, 4)
        .reshape(block, 1, -1)
    )
    pieces = upstream[:, 0].reshape(block, zhs, ys, zls, -1).transpose(2, 0, 1, 3, 4)
    pieces = lax.all_to_all(pieces.reshape(ys, block, span), "y", 0, 0, tiled=False)
    grad_full = gather_patch_blocks(pieces.transpose(1, 0, 2))
    grad_partial = jnp.einsum(
        "qgd,cd->gqc", grad_full, columns, preferred_element_type=jnp.float32
    ).astype(jnp.bfloat16)
    grad_parts = lax.all_to_all(grad_partial, "y", 0, 0, tiled=False)
    grad_rounded = grad_parts.astype(jnp.float32).sum(axis=0).astype(jnp.bfloat16)[None]
    grad_q, grad_k, grad_v = backward_heads(
        soft, queries, key_rows, value_rows, grad_rounded, head_count
    )
    return (projected, grad_q, grad_k, grad_v)


def fine_mesh(mesh):
    devices = mesh.devices
    dp, mp, seq = devices.shape
    ys = len({d.coords[1] for d in devices[:, 0, 0]}) if hasattr(devices[0, 0, 0], "coords") else dp
    shape = (dp // ys, ys, mp // 2, 2, seq)
    return Mesh(devices.reshape(shape), ("zh", "y", "x", "c", "zl"))


def solution(mesh):
    fine = fine_mesh(mesh)
    frames = ("zh", "y", "zl")
    heads = ("x", "c")
    return jax.shard_map(
        on_device,
        mesh=fine,
        in_specs=(
            P(frames, None, heads),
            P(frames, None, heads),
            P(frames, None, heads),
            P(heads, frames),
            P(heads, frames, None),
        ),
        out_specs=(
            P(heads, frames, None),
            P(frames, None, heads),
            P(frames, None, heads),
            P(frames, None, heads),
        ),
        check_vma=False,
    )
```

```python
import math

import jax
import jax.numpy as jnp
from jax import lax
from jax.sharding import Mesh, PartitionSpec as P

HEADS = 48


def split_heads(block, head_count):
    frame_count, row_count, feature_count = block.shape
    return block.reshape(frame_count, row_count, head_count, feature_count // head_count)


def soft_weights(queries, key_rows, head_count):
    split_q = split_heads(queries, head_count)
    factor = 1.0 / math.sqrt(split_q.shape[3])
    scores = (
        jnp.einsum(
            "fqhd,fkhd->fhqk",
            split_q,
            split_heads(key_rows, head_count),
            preferred_element_type=jnp.float32,
        )
        * factor
    )
    return jax.nn.softmax(scores, axis=-1)


def attend_values(soft, value_rows, head_count):
    mixed = jnp.einsum(
        "fhqk,fkhd->fqhd",
        soft.astype(jnp.bfloat16),
        split_heads(value_rows, head_count),
        preferred_element_type=jnp.float32,
    )
    frame_count, row_count = (mixed.shape[0], mixed.shape[1])
    return mixed.astype(jnp.bfloat16).reshape(frame_count, row_count, -1)


def backward_heads(soft, queries, key_rows, value_rows, grad_attended, head_count):
    split_q = split_heads(queries, head_count)
    split_k = split_heads(key_rows, head_count)
    split_v = split_heads(value_rows, head_count)
    split_g = split_heads(grad_attended, head_count)
    factor = 1.0 / math.sqrt(split_q.shape[3])
    grad_soft = jnp.einsum("fqhd,fkhd->fhqk", split_g, split_v, preferred_element_type=jnp.float32)
    inner_sum = jnp.sum(grad_soft * soft, axis=-1, keepdims=True)
    grad_scores = (soft * (grad_soft - inner_sum)).astype(jnp.bfloat16)
    grad_q = (
        jnp.einsum("fhqk,fkhd->fqhd", grad_scores, split_k, preferred_element_type=jnp.float32)
        * factor
    )
    grad_k = (
        jnp.einsum("fhqk,fqhd->fkhd", grad_scores, split_q, preferred_element_type=jnp.float32)
        * factor
    )
    grad_v = jnp.einsum(
        "fhqk,fqhd->fkhd", soft.astype(jnp.bfloat16), split_g, preferred_element_type=jnp.float32
    )
    return (
        grad_q.reshape(queries.shape),
        grad_k.reshape(key_rows.shape),
        grad_v.reshape(value_rows.shape),
    )


def swap_cores(block):
    return lax.ppermute(block, "c", [(0, 1), (1, 0)])


def gather_by_all_to_all(block, axis):
    count = lax.axis_size(axis)
    copies = jnp.broadcast_to(block[None], (count,) + block.shape)
    return lax.all_to_all(copies, axis, 0, 0, tiled=False)


def gather_patch_blocks(pieces):
    chips = lax.axis_size("x")
    mine = gather_by_all_to_all(pieces, "x")
    other = swap_cores(mine)
    first = lax.axis_index("c") == 0
    both = jnp.stack([jnp.where(first, mine, other), jnp.where(first, other, mine)], axis=1)
    return both.reshape(chips * 2 * pieces.shape[0], *pieces.shape[1:])


def sum_patch_blocks(blocks):
    core = lax.axis_index("c")
    keep = lax.dynamic_index_in_dim(blocks, core, axis=1, keepdims=False)
    send = lax.dynamic_index_in_dim(blocks, 1 - core, axis=1, keepdims=False)
    pair = (keep.astype(jnp.float32) + swap_cores(send).astype(jnp.float32)).astype(jnp.bfloat16)
    received = lax.all_to_all(pair, "x", 0, 0, tiled=False)
    return received.astype(jnp.float32).sum(axis=0).astype(jnp.bfloat16)


def on_device(queries, key_rows, value_rows, projection, upstream):
    chips, ys = lax.axis_size("x"), lax.axis_size("y")
    zhs, zls = lax.axis_size("zh"), lax.axis_size("zl")
    head_count = HEADS // (chips * 2)
    soft = soft_weights(queries, key_rows, head_count)
    attended = attend_values(soft, value_rows, head_count)
    patches, width = attended.shape[1], attended.shape[2]
    block = patches // (chips * 2)
    columns = lax.all_gather(projection, "zh", axis=1, tiled=True)
    columns = lax.all_gather(columns, "y", axis=1, tiled=True)
    span = columns.shape[1]
    group = gather_by_all_to_all(attended[0], "zl")
    tokens = group.reshape(zls, chips, 2, block, width)
    partial = jnp.einsum(
        "gxcpf,fd->xcgpd", tokens, columns, preferred_element_type=jnp.float32
    ).astype(jnp.bfloat16)
    summed = sum_patch_blocks(partial)
    own = lax.all_to_all(summed, "zl", 0, 0, tiled=False)
    projected = (
        own.reshape(zls, block, ys, zhs, span // (ys * zhs))
        .transpose(1, 3, 2, 0, 4)
        .reshape(block, 1, -1)
    )
    pieces = upstream[:, 0].reshape(block, zhs, ys, zls, -1).transpose(3, 0, 2, 1, 4)
    pieces = lax.all_to_all(pieces.reshape(zls, block, span), "zl", 0, 0, tiled=False)
    grad_full = gather_patch_blocks(pieces.transpose(1, 0, 2))
    grad_partial = jnp.einsum(
        "qgd,cd->gqc", grad_full, columns, preferred_element_type=jnp.float32
    )
    grad_parts = lax.all_to_all(grad_partial, "zl", 0, 0, tiled=False)
    grad_rounded = grad_parts.sum(axis=0).astype(jnp.bfloat16)[None]
    grad_q, grad_k, grad_v = backward_heads(
        soft, queries, key_rows, value_rows, grad_rounded, head_count
    )
    return (projected, grad_q, grad_k, grad_v)


def fine_mesh(mesh):
    devices = mesh.devices
    dp, mp, seq = devices.shape
    ys = len({d.coords[1] for d in devices[:, 0, 0]}) if hasattr(devices[0, 0, 0], "coords") else dp
    shape = (dp // ys, ys, mp // 2, 2, seq)
    return Mesh(devices.reshape(shape), ("zh", "y", "x", "c", "zl"))


def solution(mesh):
    fine = fine_mesh(mesh)
    frames = ("zh", "y", "zl")
    heads = ("x", "c")
    return jax.shard_map(
        on_device,
        mesh=fine,
        in_specs=(
            P(frames, None, heads),
            P(frames, None, heads),
            P(frames, None, heads),
            P(heads, frames),
            P(heads, frames, None),
        ),
        out_specs=(
            P(heads, frames, None),
            P(frames, None, heads),
            P(frames, None, heads),
            P(frames, None, heads),
        ),
        check_vma=False,
    )
```

```python
import math

import jax
import jax.numpy as jnp
from jax import lax
from jax.sharding import Mesh, PartitionSpec as P

HEADS = 48


def split_heads(block, head_count):
    frame_count, row_count, feature_count = block.shape
    return block.reshape(frame_count, row_count, head_count, feature_count // head_count)


def soft_weights(queries, key_rows, head_count):
    split_q = split_heads(queries, head_count)
    factor = 1.0 / math.sqrt(split_q.shape[3])
    scores = (
        jnp.einsum(
            "fqhd,fkhd->fhqk",
            split_q,
            split_heads(key_rows, head_count),
            preferred_element_type=jnp.float32,
        )
        * factor
    )
    return jax.nn.softmax(scores, axis=-1)


def attend_values(soft, value_rows, head_count):
    mixed = jnp.einsum(
        "fhqk,fkhd->fqhd",
        soft.astype(jnp.bfloat16),
        split_heads(value_rows, head_count),
        preferred_element_type=jnp.float32,
    )
    frame_count, row_count = (mixed.shape[0], mixed.shape[1])
    return mixed.astype(jnp.bfloat16).reshape(frame_count, row_count, -1)


def backward_heads(soft, queries, key_rows, value_rows, grad_attended, head_count):
    split_q = split_heads(queries, head_count)
    split_k = split_heads(key_rows, head_count)
    split_v = split_heads(value_rows, head_count)
    split_g = split_heads(grad_attended, head_count)
    factor = 1.0 / math.sqrt(split_q.shape[3])
    grad_soft = jnp.einsum("fqhd,fkhd->fhqk", split_g, split_v, preferred_element_type=jnp.float32)
    inner_sum = jnp.sum(grad_soft * soft, axis=-1, keepdims=True)
    grad_scores = (soft * (grad_soft - inner_sum)).astype(jnp.bfloat16)
    grad_q = (
        jnp.einsum("fhqk,fkhd->fqhd", grad_scores, split_k, preferred_element_type=jnp.float32)
        * factor
    )
    grad_k = (
        jnp.einsum("fhqk,fqhd->fkhd", grad_scores, split_q, preferred_element_type=jnp.float32)
        * factor
    )
    grad_v = jnp.einsum(
        "fhqk,fqhd->fkhd", soft.astype(jnp.bfloat16), split_g, preferred_element_type=jnp.float32
    )
    return (
        grad_q.reshape(queries.shape),
        grad_k.reshape(key_rows.shape),
        grad_v.reshape(value_rows.shape),
    )


def swap_cores(block):
    return lax.ppermute(block, "c", [(0, 1), (1, 0)])


def gather_by_all_to_all(block, axis):
    count = lax.axis_size(axis)
    copies = jnp.broadcast_to(block[None], (count,) + block.shape)
    return lax.all_to_all(copies, axis, 0, 0, tiled=False)


def swap_pair(block):
    return lax.ppermute(block, "zl", [(0, 1), (1, 0)])


def in_pair_order(mine, other, axis=0):
    first = lax.axis_index("zl") == 0
    return jnp.stack([jnp.where(first, mine, other), jnp.where(first, other, mine)], axis=axis)


def split_pair(blocks):
    pair = lax.axis_index("zl")
    keep = lax.dynamic_index_in_dim(blocks, pair, axis=0, keepdims=False)
    send = lax.dynamic_index_in_dim(blocks, 1 - pair, axis=0, keepdims=False)
    return keep, send


def gather_patch_blocks(pieces):
    chips = lax.axis_size("x")
    mine = gather_by_all_to_all(pieces, "x")
    other = swap_cores(mine)
    first = lax.axis_index("c") == 0
    both = jnp.stack([jnp.where(first, mine, other), jnp.where(first, other, mine)], axis=1)
    return both.reshape(chips * 2 * pieces.shape[0], *pieces.shape[1:])


def sum_patch_blocks(blocks):
    core = lax.axis_index("c")
    keep = lax.dynamic_index_in_dim(blocks, core, axis=1, keepdims=False)
    send = lax.dynamic_index_in_dim(blocks, 1 - core, axis=1, keepdims=False)
    pair = (keep.astype(jnp.float32) + swap_cores(send).astype(jnp.float32)).astype(jnp.bfloat16)
    received = lax.all_to_all(pair, "x", 0, 0, tiled=False)
    return received.astype(jnp.float32).sum(axis=0).astype(jnp.bfloat16)


def on_device(queries, key_rows, value_rows, projection, upstream):
    chips, ys = lax.axis_size("x"), lax.axis_size("y")
    zhs, zls = lax.axis_size("zh"), lax.axis_size("zl")
    head_count = HEADS // (chips * 2)
    soft = soft_weights(queries, key_rows, head_count)
    attended = attend_values(soft, value_rows, head_count)
    patches, width = attended.shape[1], attended.shape[2]
    block = patches // (chips * 2)
    columns = lax.all_gather(projection, "zh", axis=1, tiled=True)
    columns = lax.all_gather(columns, "y", axis=1, tiled=True)
    span = columns.shape[1]
    group = in_pair_order(attended[0], swap_pair(attended[0]))
    tokens = group.reshape(zls, chips, 2, block, width)
    partial = jnp.einsum(
        "gxcpf,fd->xcgpd", tokens, columns, preferred_element_type=jnp.float32
    ).astype(jnp.bfloat16)
    summed = sum_patch_blocks(partial)
    keep, send = split_pair(summed)
    own = in_pair_order(keep, swap_pair(send))
    projected = (
        own.reshape(zls, block, ys, zhs, span // (ys * zhs))
        .transpose(1, 3, 2, 0, 4)
        .reshape(block, 1, -1)
    )
    pieces = upstream[:, 0].reshape(block, zhs, ys, zls, -1).transpose(3, 0, 2, 1, 4)
    keep, send = split_pair(pieces.reshape(zls, block, span))
    pieces = in_pair_order(keep, swap_pair(send))
    grad_full = gather_patch_blocks(pieces.transpose(1, 0, 2))
    grad_partial = jnp.einsum(
        "qgd,cd->gqc", grad_full, columns, preferred_element_type=jnp.float32
    )
    keep, send = split_pair(grad_partial)
    grad_rounded = (keep + swap_pair(send)).astype(jnp.bfloat16)[None]
    grad_q, grad_k, grad_v = backward_heads(
        soft, queries, key_rows, value_rows, grad_rounded, head_count
    )
    return (projected, grad_q, grad_k, grad_v)


def fine_mesh(mesh):
    devices = mesh.devices
    dp, mp, seq = devices.shape
    ys = len({d.coords[1] for d in devices[:, 0, 0]}) if hasattr(devices[0, 0, 0], "coords") else dp
    shape = (dp // ys, ys, mp // 2, 2, seq)
    return Mesh(devices.reshape(shape), ("zh", "y", "x", "c", "zl"))


def solution(mesh):
    fine = fine_mesh(mesh)
    frames = ("zh", "y", "zl")
    heads = ("x", "c")
    return jax.shard_map(
        on_device,
        mesh=fine,
        in_specs=(
            P(frames, None, heads),
            P(frames, None, heads),
            P(frames, None, heads),
            P(heads, frames),
            P(heads, frames, None),
        ),
        out_specs=(
            P(heads, frames, None),
            P(frames, None, heads),
            P(frames, None, heads),
            P(frames, None, heads),
        ),
        check_vma=False,
    )
```

```python
import math

import jax
import jax.numpy as jnp
from jax import lax
from jax.sharding import Mesh, PartitionSpec as P

HEADS = 48


def split_heads(block, head_count):
    frame_count, row_count, feature_count = block.shape
    return block.reshape(frame_count, row_count, head_count, feature_count // head_count)


def soft_weights(queries, key_rows, head_count):
    split_q = split_heads(queries, head_count)
    factor = 1.0 / math.sqrt(split_q.shape[3])
    scores = (
        jnp.einsum(
            "fqhd,fkhd->fhqk",
            split_q,
            split_heads(key_rows, head_count),
            preferred_element_type=jnp.float32,
        )
        * factor
    )
    return jax.nn.softmax(scores, axis=-1)


def attend_values(soft, value_rows, head_count):
    mixed = jnp.einsum(
        "fhqk,fkhd->fqhd",
        soft.astype(jnp.bfloat16),
        split_heads(value_rows, head_count),
        preferred_element_type=jnp.float32,
    )
    frame_count, row_count = (mixed.shape[0], mixed.shape[1])
    return mixed.astype(jnp.bfloat16).reshape(frame_count, row_count, -1)


def backward_heads(soft, queries, key_rows, value_rows, grad_attended, head_count):
    split_q = split_heads(queries, head_count)
    split_k = split_heads(key_rows, head_count)
    split_v = split_heads(value_rows, head_count)
    split_g = split_heads(grad_attended, head_count)
    factor = 1.0 / math.sqrt(split_q.shape[3])
    grad_soft = jnp.einsum("fqhd,fkhd->fhqk", split_g, split_v, preferred_element_type=jnp.float32)
    inner_sum = jnp.sum(grad_soft * soft, axis=-1, keepdims=True)
    grad_scores = (soft * (grad_soft - inner_sum)).astype(jnp.bfloat16)
    grad_q = (
        jnp.einsum("fhqk,fkhd->fqhd", grad_scores, split_k, preferred_element_type=jnp.float32)
        * factor
    )
    grad_k = (
        jnp.einsum("fhqk,fqhd->fkhd", grad_scores, split_q, preferred_element_type=jnp.float32)
        * factor
    )
    grad_v = jnp.einsum(
        "fhqk,fqhd->fkhd", soft.astype(jnp.bfloat16), split_g, preferred_element_type=jnp.float32
    )
    return (
        grad_q.reshape(queries.shape),
        grad_k.reshape(key_rows.shape),
        grad_v.reshape(value_rows.shape),
    )


def swap_cores(block):
    return lax.ppermute(block, "c", [(0, 1), (1, 0)])


def gather_by_all_to_all(block, axis):
    count = lax.axis_size(axis)
    copies = jnp.broadcast_to(block[None], (count,) + block.shape)
    return lax.all_to_all(copies, axis, 0, 0, tiled=False)


def swap_pair(block):
    return lax.ppermute(block, "zl", [(0, 1), (1, 0)])


def in_pair_order(mine, other, axis=0):
    first = lax.axis_index("zl") == 0
    return jnp.stack([jnp.where(first, mine, other), jnp.where(first, other, mine)], axis=axis)


def split_pair(blocks):
    pair = lax.axis_index("zl")
    keep = lax.dynamic_index_in_dim(blocks, pair, axis=0, keepdims=False)
    send = lax.dynamic_index_in_dim(blocks, 1 - pair, axis=0, keepdims=False)
    return keep, send


def gather_patch_blocks(pieces):
    chips, pairs = lax.axis_size("x"), lax.axis_size("zl")
    copies = jnp.broadcast_to(pieces[None], (chips,) + pieces.shape)
    mine = lax.all_to_all(copies.reshape(chips * pairs, *pieces.shape[1:]), ("x", "zl"), 0, 0, tiled=False)
    mine = mine.reshape(chips, pairs, *pieces.shape[1:])
    other = swap_cores(mine)
    first = lax.axis_index("c") == 0
    both = jnp.stack([jnp.where(first, mine, other), jnp.where(first, other, mine)], axis=1)
    return both.transpose(0, 1, 3, 2, 4).reshape(chips * 2 * pieces.shape[1], pairs, pieces.shape[2])


def sum_patch_blocks(blocks):
    chips, pairs = lax.axis_size("x"), lax.axis_size("zl")
    core = lax.axis_index("c")
    keep = lax.dynamic_index_in_dim(blocks, core, axis=1, keepdims=False)
    send = lax.dynamic_index_in_dim(blocks, 1 - core, axis=1, keepdims=False)
    pair = (keep.astype(jnp.float32) + swap_cores(send).astype(jnp.float32)).astype(jnp.bfloat16)
    pair = pair.reshape(chips * pairs, *pair.shape[2:])
    received = lax.all_to_all(pair, ("x", "zl"), 0, 0, tiled=False)
    received = received.reshape(chips, pairs, *pair.shape[1:])
    return received.astype(jnp.float32).sum(axis=0).astype(jnp.bfloat16)


def on_device(queries, key_rows, value_rows, projection, upstream):
    chips, ys = lax.axis_size("x"), lax.axis_size("y")
    zhs, zls = lax.axis_size("zh"), lax.axis_size("zl")
    head_count = HEADS // (chips * 2)
    soft = soft_weights(queries, key_rows, head_count)
    attended = attend_values(soft, value_rows, head_count)
    patches, width = attended.shape[1], attended.shape[2]
    block = patches // (chips * 2)
    columns = lax.all_gather(projection, "zh", axis=1, tiled=True)
    columns = lax.all_gather(columns, "y", axis=1, tiled=True)
    span = columns.shape[1]
    group = in_pair_order(attended[0], swap_pair(attended[0]))
    tokens = group.reshape(zls, chips, 2, block, width)
    partial = jnp.einsum(
        "gxcpf,fd->xcgpd", tokens, columns, preferred_element_type=jnp.float32
    ).astype(jnp.bfloat16)
    own = sum_patch_blocks(partial)
    projected = (
        own.reshape(zls, block, ys, zhs, span // (ys * zhs))
        .transpose(1, 3, 2, 0, 4)
        .reshape(block, 1, -1)
    )
    pieces = upstream[:, 0].reshape(block, zhs, ys, zls, -1).transpose(3, 0, 2, 1, 4)
    grad_full = gather_patch_blocks(pieces.reshape(zls, block, span))
    grad_partial = jnp.einsum(
        "qgd,cd->gqc", grad_full, columns, preferred_element_type=jnp.float32
    )
    keep, send = split_pair(grad_partial)
    grad_rounded = (keep + swap_pair(send)).astype(jnp.bfloat16)[None]
    grad_q, grad_k, grad_v = backward_heads(
        soft, queries, key_rows, value_rows, grad_rounded, head_count
    )
    return (projected, grad_q, grad_k, grad_v)


def fine_mesh(mesh):
    devices = mesh.devices
    dp, mp, seq = devices.shape
    ys = len({d.coords[1] for d in devices[:, 0, 0]}) if hasattr(devices[0, 0, 0], "coords") else dp
    shape = (dp // ys, ys, mp // 2, 2, seq)
    return Mesh(devices.reshape(shape), ("zh", "y", "x", "c", "zl"))


def solution(mesh):
    fine = fine_mesh(mesh)
    frames = ("zh", "y", "zl")
    heads = ("x", "c")
    return jax.shard_map(
        on_device,
        mesh=fine,
        in_specs=(
            P(frames, None, heads),
            P(frames, None, heads),
            P(frames, None, heads),
            P(heads, frames),
            P(heads, frames, None),
        ),
        out_specs=(
            P(heads, frames, None),
            P(frames, None, heads),
            P(frames, None, heads),
            P(frames, None, heads),
        ),
        check_vma=False,
    )
```

```python
import math

import jax
import jax.numpy as jnp
from jax import lax
from jax.sharding import Mesh, PartitionSpec as P

HEADS = 48


def split_heads(block, head_count):
    frame_count, row_count, feature_count = block.shape
    return block.reshape(frame_count, row_count, head_count, feature_count // head_count)


def soft_weights(queries, key_rows, head_count):
    split_q = split_heads(queries, head_count)
    factor = 1.0 / math.sqrt(split_q.shape[3])
    scores = (
        jnp.einsum(
            "fqhd,fkhd->fhqk",
            split_q,
            split_heads(key_rows, head_count),
            preferred_element_type=jnp.float32,
        )
        * factor
    )
    return jax.nn.softmax(scores, axis=-1)


def attend_values(soft, value_rows, head_count):
    mixed = jnp.einsum(
        "fhqk,fkhd->fqhd",
        soft.astype(jnp.bfloat16),
        split_heads(value_rows, head_count),
        preferred_element_type=jnp.float32,
    )
    frame_count, row_count = (mixed.shape[0], mixed.shape[1])
    return mixed.astype(jnp.bfloat16).reshape(frame_count, row_count, -1)


def backward_heads(soft, queries, key_rows, value_rows, grad_attended, head_count):
    split_q = split_heads(queries, head_count)
    split_k = split_heads(key_rows, head_count)
    split_v = split_heads(value_rows, head_count)
    split_g = split_heads(grad_attended, head_count)
    factor = 1.0 / math.sqrt(split_q.shape[3])
    grad_soft = jnp.einsum("fqhd,fkhd->fhqk", split_g, split_v, preferred_element_type=jnp.float32)
    inner_sum = jnp.sum(grad_soft * soft, axis=-1, keepdims=True)
    grad_scores = (soft * (grad_soft - inner_sum)).astype(jnp.bfloat16)
    grad_q = (
        jnp.einsum("fhqk,fkhd->fqhd", grad_scores, split_k, preferred_element_type=jnp.float32)
        * factor
    )
    grad_k = (
        jnp.einsum("fhqk,fqhd->fkhd", grad_scores, split_q, preferred_element_type=jnp.float32)
        * factor
    )
    grad_v = jnp.einsum(
        "fhqk,fqhd->fkhd", soft.astype(jnp.bfloat16), split_g, preferred_element_type=jnp.float32
    )
    return (
        grad_q.reshape(queries.shape),
        grad_k.reshape(key_rows.shape),
        grad_v.reshape(value_rows.shape),
    )


def swap_cores(block):
    return lax.ppermute(block, "c", [(0, 1), (1, 0)])


def gather_by_all_to_all(block, axis):
    count = lax.axis_size(axis)
    copies = jnp.broadcast_to(block[None], (count,) + block.shape)
    return lax.all_to_all(copies, axis, 0, 0, tiled=False)


def swap_pair(block):
    return lax.ppermute(block, "zl", [(0, 1), (1, 0)])


def in_pair_order(mine, other, axis=0):
    first = lax.axis_index("zl") == 0
    return jnp.stack([jnp.where(first, mine, other), jnp.where(first, other, mine)], axis=axis)


def split_pair(blocks):
    pair = lax.axis_index("zl")
    keep = lax.dynamic_index_in_dim(blocks, pair, axis=0, keepdims=False)
    send = lax.dynamic_index_in_dim(blocks, 1 - pair, axis=0, keepdims=False)
    return keep, send


def gather_patch_blocks(pieces):
    chips, pairs = lax.axis_size("x"), lax.axis_size("zl")
    copies = jnp.broadcast_to(pieces[None], (chips,) + pieces.shape)
    mine = lax.all_to_all(copies.reshape(chips * pairs, *pieces.shape[1:]), ("x", "zl"), 0, 0, tiled=False)
    mine = mine.reshape(chips, pairs, *pieces.shape[1:])
    other = swap_cores(mine)
    first = lax.axis_index("c") == 0
    both = jnp.stack([jnp.where(first, mine, other), jnp.where(first, other, mine)], axis=1)
    return both.transpose(0, 1, 3, 2, 4).reshape(chips * 2 * pieces.shape[1], pairs, pieces.shape[2])


def sum_patch_blocks(blocks):
    chips, pairs = lax.axis_size("x"), lax.axis_size("zl")
    core = lax.axis_index("c")
    keep = lax.dynamic_index_in_dim(blocks, core, axis=1, keepdims=False)
    send = lax.dynamic_index_in_dim(blocks, 1 - core, axis=1, keepdims=False)
    pair = (keep.astype(jnp.float32) + swap_cores(send).astype(jnp.float32)).astype(jnp.bfloat16)
    pair = pair.reshape(chips * pairs, *pair.shape[2:])
    received = lax.all_to_all(pair, ("x", "zl"), 0, 0, tiled=False)
    received = received.reshape(chips, pairs, *pair.shape[1:])
    return received.astype(jnp.float32).sum(axis=0).astype(jnp.bfloat16)


def on_device(queries, key_rows, value_rows, projection, upstream):
    chips, ys = lax.axis_size("x"), lax.axis_size("y")
    zhs, zls = lax.axis_size("zh"), lax.axis_size("zl")
    head_count = HEADS // (chips * 2)
    soft = soft_weights(queries, key_rows, head_count)
    attended = attend_values(soft, value_rows, head_count)
    patches, width = attended.shape[1], attended.shape[2]
    block = patches // (chips * 2)
    columns = lax.all_gather(projection, "zh", axis=1, tiled=True)
    columns = lax.all_gather(columns, "y", axis=1, tiled=True)
    span = columns.shape[1]
    group = in_pair_order(attended[0], swap_pair(attended[0]))
    tokens = group.reshape(zls, chips, 2, block, width)
    partial = jnp.einsum(
        "gxcpf,fd->xcgpd", tokens, columns, preferred_element_type=jnp.float32
    ).astype(jnp.bfloat16)
    own = sum_patch_blocks(partial)
    projected = (
        own.reshape(zls, block, ys, zhs, span // (ys * zhs))
        .transpose(1, 3, 2, 0, 4)
        .reshape(block, 1, -1)
    )
    pieces = upstream[:, 0].reshape(block, zhs, ys, zls, -1).transpose(3, 0, 2, 1, 4)
    grad_full = gather_patch_blocks(pieces.reshape(zls, block, span))
    grad_partial = jnp.einsum(
        "qgd,cd->gqc", grad_full, columns, preferred_element_type=jnp.float32
    )
    keep, send = split_pair(grad_partial)
    arrived = swap_pair(send.astype(jnp.bfloat16)).astype(jnp.float32)
    grad_rounded = (keep + arrived).astype(jnp.bfloat16)[None]
    grad_q, grad_k, grad_v = backward_heads(
        soft, queries, key_rows, value_rows, grad_rounded, head_count
    )
    return (projected, grad_q, grad_k, grad_v)


def fine_mesh(mesh):
    devices = mesh.devices
    dp, mp, seq = devices.shape
    ys = len({d.coords[1] for d in devices[:, 0, 0]}) if hasattr(devices[0, 0, 0], "coords") else dp
    shape = (dp // ys, ys, mp // 2, 2, seq)
    return Mesh(devices.reshape(shape), ("zh", "y", "x", "c", "zl"))


def solution(mesh):
    fine = fine_mesh(mesh)
    frames = ("zh", "y", "zl")
    heads = ("x", "c")
    return jax.shard_map(
        on_device,
        mesh=fine,
        in_specs=(
            P(frames, None, heads),
            P(frames, None, heads),
            P(frames, None, heads),
            P(heads, frames),
            P(heads, frames, None),
        ),
        out_specs=(
            P(heads, frames, None),
            P(frames, None, heads),
            P(frames, None, heads),
            P(frames, None, heads),
        ),
        check_vma=False,
    )
```

```python
import math

import jax
import jax.numpy as jnp
from jax import lax
from jax.sharding import Mesh, PartitionSpec as P

HEADS = 48


def split_heads(block, head_count):
    frame_count, row_count, feature_count = block.shape
    return block.reshape(frame_count, row_count, head_count, feature_count // head_count)


def soft_weights(queries, key_rows, head_count):
    split_q = split_heads(queries, head_count)
    factor = 1.0 / math.sqrt(split_q.shape[3])
    scores = (
        jnp.einsum(
            "fqhd,fkhd->fhqk",
            split_q,
            split_heads(key_rows, head_count),
            preferred_element_type=jnp.float32,
        )
        * factor
    )
    return jax.nn.softmax(scores, axis=-1)


def attend_values(soft, value_rows, head_count):
    mixed = jnp.einsum(
        "fhqk,fkhd->fqhd",
        soft.astype(jnp.bfloat16),
        split_heads(value_rows, head_count),
        preferred_element_type=jnp.float32,
    )
    frame_count, row_count = (mixed.shape[0], mixed.shape[1])
    return mixed.astype(jnp.bfloat16).reshape(frame_count, row_count, -1)


def backward_heads(soft, queries, key_rows, value_rows, grad_attended, head_count):
    split_q = split_heads(queries, head_count)
    split_k = split_heads(key_rows, head_count)
    split_v = split_heads(value_rows, head_count)
    split_g = split_heads(grad_attended, head_count)
    factor = 1.0 / math.sqrt(split_q.shape[3])
    grad_soft = jnp.einsum("fqhd,fkhd->fhqk", split_g, split_v, preferred_element_type=jnp.float32)
    inner_sum = jnp.sum(grad_soft * soft, axis=-1, keepdims=True)
    grad_scores = (soft * (grad_soft - inner_sum)).astype(jnp.bfloat16)
    grad_q = (
        jnp.einsum("fhqk,fkhd->fqhd", grad_scores, split_k, preferred_element_type=jnp.float32)
        * factor
    )
    grad_k = (
        jnp.einsum("fhqk,fqhd->fkhd", grad_scores, split_q, preferred_element_type=jnp.float32)
        * factor
    )
    grad_v = jnp.einsum(
        "fhqk,fqhd->fkhd", soft.astype(jnp.bfloat16), split_g, preferred_element_type=jnp.float32
    )
    return (
        grad_q.reshape(queries.shape),
        grad_k.reshape(key_rows.shape),
        grad_v.reshape(value_rows.shape),
    )


def swap_cores(block):
    return lax.ppermute(block, "c", [(0, 1), (1, 0)])


def gather_by_all_to_all(block, axis):
    count = lax.axis_size(axis)
    copies = jnp.broadcast_to(block[None], (count,) + block.shape)
    return lax.all_to_all(copies, axis, 0, 0, tiled=False)


def swap_pair(block):
    return lax.ppermute(block, "zl", [(0, 1), (1, 0)])


def in_pair_order(mine, other, axis=0):
    first = lax.axis_index("zl") == 0
    return jnp.stack([jnp.where(first, mine, other), jnp.where(first, other, mine)], axis=axis)


def split_pair(blocks):
    pair = lax.axis_index("zl")
    keep = lax.dynamic_index_in_dim(blocks, pair, axis=0, keepdims=False)
    send = lax.dynamic_index_in_dim(blocks, 1 - pair, axis=0, keepdims=False)
    return keep, send


def gather_patch_blocks(pieces):
    chips, pairs = lax.axis_size("x"), lax.axis_size("zl")
    copies = jnp.broadcast_to(pieces[None], (chips,) + pieces.shape)
    mine = lax.all_to_all(copies.reshape(chips * pairs, *pieces.shape[1:]), ("x", "zl"), 0, 0, tiled=False)
    mine = mine.reshape(chips, pairs, *pieces.shape[1:])
    other = swap_cores(mine)
    first = lax.axis_index("c") == 0
    both = jnp.stack([jnp.where(first, mine, other), jnp.where(first, other, mine)], axis=1)
    return both.transpose(0, 1, 3, 2, 4).reshape(chips * 2 * pieces.shape[1], pairs, pieces.shape[2])


def sum_patch_blocks(send, keep):
    chips, pairs = lax.axis_size("x"), lax.axis_size("zl")
    pair = (keep.astype(jnp.float32) + swap_cores(send).astype(jnp.float32)).astype(jnp.bfloat16)
    pair = pair.reshape(chips * pairs, *pair.shape[2:])
    received = lax.all_to_all(pair, ("x", "zl"), 0, 0, tiled=False)
    received = received.reshape(chips, pairs, *pair.shape[1:])
    return received.astype(jnp.float32).sum(axis=0).astype(jnp.bfloat16)


def on_device(queries, key_rows, value_rows, projection, upstream):
    chips, ys = lax.axis_size("x"), lax.axis_size("y")
    zhs, zls = lax.axis_size("zh"), lax.axis_size("zl")
    head_count = HEADS // (chips * 2)
    soft = soft_weights(queries, key_rows, head_count)
    attended = attend_values(soft, value_rows, head_count)
    patches, width = attended.shape[1], attended.shape[2]
    block = patches // (chips * 2)
    columns = lax.all_gather(projection, "zh", axis=1, tiled=True)
    columns = lax.all_gather(columns, "y", axis=1, tiled=True)
    span = columns.shape[1]
    group = in_pair_order(attended[0], swap_pair(attended[0]))
    tokens = group.reshape(zls, chips, 2, block, width)
    core = lax.axis_index("c")
    halves = [
        jnp.einsum(
            "gxpf,fd->xgpd",
            lax.dynamic_index_in_dim(tokens, pick, axis=2, keepdims=False),
            columns,
            preferred_element_type=jnp.float32,
        ).astype(jnp.bfloat16)
        for pick in (1 - core, core)
    ]
    own = sum_patch_blocks(*halves)
    projected = (
        own.reshape(zls, block, ys, zhs, span // (ys * zhs))
        .transpose(1, 3, 2, 0, 4)
        .reshape(block, 1, -1)
    )
    pieces = upstream[:, 0].reshape(block, zhs, ys, zls, -1).transpose(3, 0, 2, 1, 4)
    grad_full = gather_patch_blocks(pieces.reshape(zls, block, span))
    grad_partial = jnp.einsum(
        "qgd,cd->gqc", grad_full, columns, preferred_element_type=jnp.float32
    )
    keep, send = split_pair(grad_partial)
    grad_rounded = (keep + swap_pair(send)).astype(jnp.bfloat16)[None]
    grad_q, grad_k, grad_v = backward_heads(
        soft, queries, key_rows, value_rows, grad_rounded, head_count
    )
    return (projected, grad_q, grad_k, grad_v)


def fine_mesh(mesh):
    devices = mesh.devices
    dp, mp, seq = devices.shape
    ys = len({d.coords[1] for d in devices[:, 0, 0]}) if hasattr(devices[0, 0, 0], "coords") else dp
    shape = (dp // ys, ys, mp // 2, 2, seq)
    return Mesh(devices.reshape(shape), ("zh", "y", "x", "c", "zl"))


def solution(mesh):
    fine = fine_mesh(mesh)
    frames = ("zh", "y", "zl")
    heads = ("x", "c")
    return jax.shard_map(
        on_device,
        mesh=fine,
        in_specs=(
            P(frames, None, heads),
            P(frames, None, heads),
            P(frames, None, heads),
            P(heads, frames),
            P(heads, frames, None),
        ),
        out_specs=(
            P(heads, frames, None),
            P(frames, None, heads),
            P(frames, None, heads),
            P(frames, None, heads),
        ),
        check_vma=False,
    )
```

```python
import math

import jax
import jax.numpy as jnp
from jax import lax
from jax.sharding import Mesh, PartitionSpec as P

HEADS = 48


def split_heads(block, head_count):
    frame_count, row_count, feature_count = block.shape
    return block.reshape(frame_count, row_count, head_count, feature_count // head_count)


def soft_weights(queries, key_rows, head_count):
    split_q = split_heads(queries, head_count)
    factor = 1.0 / math.sqrt(split_q.shape[3])
    scores = (
        jnp.einsum(
            "fqhd,fkhd->fhqk",
            split_q,
            split_heads(key_rows, head_count),
            preferred_element_type=jnp.float32,
        )
        * factor
    )
    return jax.nn.softmax(scores, axis=-1)


def attend_values(soft, value_rows, head_count):
    mixed = jnp.einsum(
        "fhqk,fkhd->fqhd",
        soft.astype(jnp.bfloat16),
        split_heads(value_rows, head_count),
        preferred_element_type=jnp.float32,
    )
    frame_count, row_count = (mixed.shape[0], mixed.shape[1])
    return mixed.astype(jnp.bfloat16).reshape(frame_count, row_count, -1)


def backward_heads(soft, queries, key_rows, value_rows, grad_attended, head_count):
    split_q = split_heads(queries, head_count)
    split_k = split_heads(key_rows, head_count)
    split_v = split_heads(value_rows, head_count)
    split_g = split_heads(grad_attended, head_count)
    factor = 1.0 / math.sqrt(split_q.shape[3])
    grad_soft = jnp.einsum("fqhd,fkhd->fhqk", split_g, split_v, preferred_element_type=jnp.float32)
    inner_sum = jnp.sum(grad_soft * soft, axis=-1, keepdims=True)
    grad_scores = (soft * (grad_soft - inner_sum)).astype(jnp.bfloat16)
    grad_q = (
        jnp.einsum("fhqk,fkhd->fqhd", grad_scores, split_k, preferred_element_type=jnp.float32)
        * factor
    )
    grad_k = (
        jnp.einsum("fhqk,fqhd->fkhd", grad_scores, split_q, preferred_element_type=jnp.float32)
        * factor
    )
    grad_v = jnp.einsum(
        "fhqk,fqhd->fkhd", soft.astype(jnp.bfloat16), split_g, preferred_element_type=jnp.float32
    )
    return (
        grad_q.reshape(queries.shape),
        grad_k.reshape(key_rows.shape),
        grad_v.reshape(value_rows.shape),
    )


def swap_cores(block):
    return lax.ppermute(block, "c", [(0, 1), (1, 0)])


def gather_by_all_to_all(block, axis):
    count = lax.axis_size(axis)
    copies = jnp.broadcast_to(block[None], (count,) + block.shape)
    return lax.all_to_all(copies, axis, 0, 0, tiled=False)


def swap_pair(block):
    return lax.ppermute(block, "zl", [(0, 1), (1, 0)])


def in_pair_order(mine, other, axis=0):
    first = lax.axis_index("zl") == 0
    return jnp.stack([jnp.where(first, mine, other), jnp.where(first, other, mine)], axis=axis)


def split_pair(blocks):
    pair = lax.axis_index("zl")
    keep = lax.dynamic_index_in_dim(blocks, pair, axis=0, keepdims=False)
    send = lax.dynamic_index_in_dim(blocks, 1 - pair, axis=0, keepdims=False)
    return keep, send


def gather_patch_blocks(pieces):
    chips, pairs = lax.axis_size("x"), lax.axis_size("zl")
    copies = jnp.broadcast_to(pieces[None], (chips,) + pieces.shape)
    mine = lax.all_to_all(copies.reshape(chips * pairs, *pieces.shape[1:]), ("x", "zl"), 0, 0, tiled=False)
    mine = mine.reshape(chips, pairs, *pieces.shape[1:])
    other = swap_cores(mine)
    first = lax.axis_index("c") == 0
    both = jnp.stack([jnp.where(first, mine, other), jnp.where(first, other, mine)], axis=1)
    return both.transpose(0, 1, 3, 2, 4).reshape(chips * 2 * pieces.shape[1], pairs, pieces.shape[2])


def sum_patch_blocks(blocks):
    chips, pairs = lax.axis_size("x"), lax.axis_size("zl")
    core = lax.axis_index("c")
    keep = lax.dynamic_index_in_dim(blocks, core, axis=1, keepdims=False)
    send = lax.dynamic_index_in_dim(blocks, 1 - core, axis=1, keepdims=False)
    pair = (keep.astype(jnp.float32) + swap_cores(send).astype(jnp.float32)).astype(jnp.bfloat16)
    pair = pair.reshape(chips * pairs, *pair.shape[2:])
    received = lax.all_to_all(pair, ("x", "zl"), 0, 0, tiled=False)
    received = received.reshape(chips, pairs, *pair.shape[1:])
    return received.astype(jnp.float32).sum(axis=0).astype(jnp.bfloat16)


def ring_gather_columns(block, axis):
    count = lax.axis_size(axis)
    ahead = [(i, (i + 1) % count) for i in range(count)]
    behind = [(i, (i - 1) % count) for i in range(count)]
    before, after = [], []
    from_behind = from_ahead = block
    for step in range(count // 2):
        from_behind = lax.ppermute(from_behind, axis, ahead)
        before.append(from_behind)
        if step < (count - 1) // 2:
            from_ahead = lax.ppermute(from_ahead, axis, behind)
            after.append(from_ahead)
    ordered = jnp.stack(before[::-1] + [block] + after, axis=0)
    shift = lax.axis_index(axis) - count // 2
    placed = jnp.roll(ordered, shift, axis=0)
    return placed.transpose(1, 0, 2).reshape(block.shape[0], -1)


def on_device(queries, key_rows, value_rows, projection, upstream):
    chips, ys = lax.axis_size("x"), lax.axis_size("y")
    zhs, zls = lax.axis_size("zh"), lax.axis_size("zl")
    head_count = HEADS // (chips * 2)
    soft = soft_weights(queries, key_rows, head_count)
    attended = attend_values(soft, value_rows, head_count)
    patches, width = attended.shape[1], attended.shape[2]
    block = patches // (chips * 2)
    columns = lax.all_gather(projection, "zh", axis=1, tiled=True)
    columns = ring_gather_columns(columns, "y")
    span = columns.shape[1]
    group = in_pair_order(attended[0], swap_pair(attended[0]))
    tokens = group.reshape(zls, chips, 2, block, width)
    partial = jnp.einsum(
        "gxcpf,fd->xcgpd", tokens, columns, preferred_element_type=jnp.float32
    ).astype(jnp.bfloat16)
    own = sum_patch_blocks(partial)
    projected = (
        own.reshape(zls, block, ys, zhs, span // (ys * zhs))
        .transpose(1, 3, 2, 0, 4)
        .reshape(block, 1, -1)
    )
    pieces = upstream[:, 0].reshape(block, zhs, ys, zls, -1).transpose(3, 0, 2, 1, 4)
    grad_full = gather_patch_blocks(pieces.reshape(zls, block, span))
    grad_partial = jnp.einsum(
        "qgd,cd->gqc", grad_full, columns, preferred_element_type=jnp.float32
    )
    keep, send = split_pair(grad_partial)
    grad_rounded = (keep + swap_pair(send)).astype(jnp.bfloat16)[None]
    grad_q, grad_k, grad_v = backward_heads(
        soft, queries, key_rows, value_rows, grad_rounded, head_count
    )
    return (projected, grad_q, grad_k, grad_v)


def fine_mesh(mesh):
    devices = mesh.devices
    dp, mp, seq = devices.shape
    ys = len({d.coords[1] for d in devices[:, 0, 0]}) if hasattr(devices[0, 0, 0], "coords") else dp
    shape = (dp // ys, ys, mp // 2, 2, seq)
    return Mesh(devices.reshape(shape), ("zh", "y", "x", "c", "zl"))


def solution(mesh):
    fine = fine_mesh(mesh)
    frames = ("zh", "y", "zl")
    heads = ("x", "c")
    return jax.shard_map(
        on_device,
        mesh=fine,
        in_specs=(
            P(frames, None, heads),
            P(frames, None, heads),
            P(frames, None, heads),
            P(heads, frames),
            P(heads, frames, None),
        ),
        out_specs=(
            P(heads, frames, None),
            P(frames, None, heads),
            P(frames, None, heads),
            P(frames, None, heads),
        ),
        check_vma=False,
    )
```

```python
import math

import jax
import jax.numpy as jnp
from jax import lax
from jax.sharding import Mesh, PartitionSpec as P

HEADS = 48


def split_heads(block, head_count):
    frame_count, row_count, feature_count = block.shape
    return block.reshape(frame_count, row_count, head_count, feature_count // head_count)


def soft_weights(queries, key_rows, head_count):
    split_q = split_heads(queries, head_count)
    factor = 1.0 / math.sqrt(split_q.shape[3])
    scores = (
        jnp.einsum(
            "fqhd,fkhd->fhqk",
            split_q,
            split_heads(key_rows, head_count),
            preferred_element_type=jnp.float32,
        )
        * factor
    )
    return jax.nn.softmax(scores, axis=-1)


def attend_values(soft, value_rows, head_count):
    mixed = jnp.einsum(
        "fhqk,fkhd->fqhd",
        soft.astype(jnp.bfloat16),
        split_heads(value_rows, head_count),
        preferred_element_type=jnp.float32,
    )
    frame_count, row_count = (mixed.shape[0], mixed.shape[1])
    return mixed.astype(jnp.bfloat16).reshape(frame_count, row_count, -1)


def backward_heads(soft, queries, key_rows, value_rows, grad_attended, head_count):
    split_q = split_heads(queries, head_count)
    split_k = split_heads(key_rows, head_count)
    split_v = split_heads(value_rows, head_count)
    split_g = split_heads(grad_attended, head_count)
    factor = 1.0 / math.sqrt(split_q.shape[3])
    grad_soft = jnp.einsum("fqhd,fkhd->fhqk", split_g, split_v, preferred_element_type=jnp.float32)
    inner_sum = jnp.sum(grad_soft * soft, axis=-1, keepdims=True)
    grad_scores = (soft * (grad_soft - inner_sum)).astype(jnp.bfloat16)
    grad_q = (
        jnp.einsum("fhqk,fkhd->fqhd", grad_scores, split_k, preferred_element_type=jnp.float32)
        * factor
    )
    grad_k = (
        jnp.einsum("fhqk,fqhd->fkhd", grad_scores, split_q, preferred_element_type=jnp.float32)
        * factor
    )
    grad_v = jnp.einsum(
        "fhqk,fqhd->fkhd", soft.astype(jnp.bfloat16), split_g, preferred_element_type=jnp.float32
    )
    return (
        grad_q.reshape(queries.shape),
        grad_k.reshape(key_rows.shape),
        grad_v.reshape(value_rows.shape),
    )


def swap_cores(block):
    return lax.ppermute(block, "c", [(0, 1), (1, 0)])


def gather_by_all_to_all(block, axis):
    count = lax.axis_size(axis)
    copies = jnp.broadcast_to(block[None], (count,) + block.shape)
    return lax.all_to_all(copies, axis, 0, 0, tiled=False)


def swap_pair(block):
    return lax.ppermute(block, "zl", [(0, 1), (1, 0)])


def in_pair_order(mine, other, axis=0):
    first = lax.axis_index("zl") == 0
    return jnp.stack([jnp.where(first, mine, other), jnp.where(first, other, mine)], axis=axis)


def split_pair(blocks):
    pair = lax.axis_index("zl")
    keep = lax.dynamic_index_in_dim(blocks, pair, axis=0, keepdims=False)
    send = lax.dynamic_index_in_dim(blocks, 1 - pair, axis=0, keepdims=False)
    return keep, send


def gather_patch_blocks(pieces):
    chips, pairs = lax.axis_size("x"), lax.axis_size("zl")
    copies = jnp.broadcast_to(pieces[None], (chips,) + pieces.shape)
    mine = lax.all_to_all(copies.reshape(chips * pairs, *pieces.shape[1:]), ("x", "zl"), 0, 0, tiled=False)
    mine = mine.reshape(chips, pairs, *pieces.shape[1:])
    other = swap_cores(mine)
    first = lax.axis_index("c") == 0
    both = jnp.stack([jnp.where(first, mine, other), jnp.where(first, other, mine)], axis=1)
    return both.transpose(0, 1, 3, 2, 4).reshape(chips * 2 * pieces.shape[1], pairs, pieces.shape[2])


def sum_patch_blocks(blocks):
    chips, pairs = lax.axis_size("x"), lax.axis_size("zl")
    core = lax.axis_index("c")
    keep = lax.dynamic_index_in_dim(blocks, core, axis=1, keepdims=False)
    send = lax.dynamic_index_in_dim(blocks, 1 - core, axis=1, keepdims=False)
    pair = (keep.astype(jnp.float32) + swap_cores(send).astype(jnp.float32)).astype(jnp.bfloat16)
    pair = pair.reshape(chips * pairs, *pair.shape[2:])
    received = lax.all_to_all(pair, ("x", "zl"), 0, 0, tiled=False)
    received = received.reshape(chips, pairs, *pair.shape[1:])
    return received.astype(jnp.float32).sum(axis=0).astype(jnp.bfloat16)


def ring_gather_columns(block, axis):
    count = lax.axis_size(axis)
    ahead = [(i, (i + 1) % count) for i in range(count)]
    behind = [(i, (i - 1) % count) for i in range(count)]
    before, after = [], []
    from_behind = from_ahead = block
    for step in range(count // 2):
        from_behind = lax.ppermute(from_behind, axis, ahead)
        before.append(from_behind)
        if step < (count - 1) // 2:
            from_ahead = lax.ppermute(from_ahead, axis, behind)
            after.append(from_ahead)
    ordered = jnp.stack(before[::-1] + [block] + after, axis=0)
    shift = lax.axis_index(axis) - count // 2
    placed = jnp.roll(ordered, shift, axis=0)
    return placed.transpose(1, 0, 2).reshape(block.shape[0], -1)


def on_device(queries, key_rows, value_rows, projection, upstream):
    chips, ys = lax.axis_size("x"), lax.axis_size("y")
    zhs, zls = lax.axis_size("zh"), lax.axis_size("zl")
    head_count = HEADS // (chips * 2)
    soft = soft_weights(queries, key_rows, head_count)
    attended = attend_values(soft, value_rows, head_count)
    patches, width = attended.shape[1], attended.shape[2]
    block = patches // (chips * 2)
    columns = ring_gather_columns(projection, "zh")
    columns = ring_gather_columns(columns, "y")
    span = columns.shape[1]
    group = in_pair_order(attended[0], swap_pair(attended[0]))
    tokens = group.reshape(zls, chips, 2, block, width)
    partial = jnp.einsum(
        "gxcpf,fd->xcgpd", tokens, columns, preferred_element_type=jnp.float32
    ).astype(jnp.bfloat16)
    own = sum_patch_blocks(partial)
    projected = (
        own.reshape(zls, block, ys, zhs, span // (ys * zhs))
        .transpose(1, 3, 2, 0, 4)
        .reshape(block, 1, -1)
    )
    pieces = upstream[:, 0].reshape(block, zhs, ys, zls, -1).transpose(3, 0, 2, 1, 4)
    grad_full = gather_patch_blocks(pieces.reshape(zls, block, span))
    grad_partial = jnp.einsum(
        "qgd,cd->gqc", grad_full, columns, preferred_element_type=jnp.float32
    )
    keep, send = split_pair(grad_partial)
    grad_rounded = (keep + swap_pair(send)).astype(jnp.bfloat16)[None]
    grad_q, grad_k, grad_v = backward_heads(
        soft, queries, key_rows, value_rows, grad_rounded, head_count
    )
    return (projected, grad_q, grad_k, grad_v)


def fine_mesh(mesh):
    devices = mesh.devices
    dp, mp, seq = devices.shape
    ys = len({d.coords[1] for d in devices[:, 0, 0]}) if hasattr(devices[0, 0, 0], "coords") else dp
    shape = (dp // ys, ys, mp // 2, 2, seq)
    return Mesh(devices.reshape(shape), ("zh", "y", "x", "c", "zl"))


def solution(mesh):
    fine = fine_mesh(mesh)
    frames = ("zh", "y", "zl")
    heads = ("x", "c")
    return jax.shard_map(
        on_device,
        mesh=fine,
        in_specs=(
            P(frames, None, heads),
            P(frames, None, heads),
            P(frames, None, heads),
            P(heads, frames),
            P(heads, frames, None),
        ),
        out_specs=(
            P(heads, frames, None),
            P(frames, None, heads),
            P(frames, None, heads),
            P(frames, None, heads),
        ),
        check_vma=False,
    )
```
